1024 devices in a mesh: seq: 64 (over y_hi, z), chan: 16 (over y_lo, x, core).
Axes of the slice: x: 4, y: 8 (y_hi: 4, y_lo: 2; y = y_hi * 2 + y_lo), z: 16, core: 2. Of those that a mesh axis runs over, the one named last changes fastest.
Arguments:
- query_gate: float32 [64, 524288], P('chan', 'seq'), may hold values from -6 to 6
- key_gate: float32 [64, 524288], P('chan', 'seq'), may hold values from -6 to 6
- value_input: float32 [64, 524288], P('chan', 'seq'), may hold values from -6 to 6
- filter_taps: float32 [4, 524288], P(None, ('seq', 'chan')), may hold values from -2 to 2
- cotangent: float32 [64, 524288], P('chan', 'seq'), may hold values from -6 to 6
Outputs:
- query_grad: float32 [64, 524288], P('chan', 'seq')
- key_grad: float32 [64, 524288], P('chan', 'seq')
- value_grad: float32 [64, 524288], P('chan', 'seq')
The draws below stay inside these ranges and needn't reach their ends.
All inputs are finite; a program needn't handle non-finite values.
Results may differ from the reference program's by a relative error of at most 0.00013.
Values sent between devices are 32-bit elements; how exact they have to be, the bound alone decides.
No kernel may reach another device: no remote copies, remote signals or barrier semaphores. Data moves between devices by JAX's collectives and lax.ppermute only.
A program may use at most 32 MiB of HBM per device.

```python
import math
import jax
import jax.numpy as jnp
from jax import lax

FILTERS = 4
CHANNELS = 64
LENGTH = 524288


def draw_filter_taps(key, part):
    noise_seed, rate_seed = jax.random.split(key)
    lag_index = jnp.arange(LENGTH, dtype=jnp.float32)[None, :]
    decay_span = jnp.exp(jax.random.uniform(rate_seed, (FILTERS, 1), jnp.float32, math.log(4.0), math.log(64.0)))
    noise_draw = jnp.clip(jax.random.normal(noise_seed, (FILTERS, LENGTH), jnp.float32), -6.0, 6.0)
    far_level = 1.2 / math.sqrt(LENGTH)
    return noise_draw * (0.3 * jnp.exp(-lag_index / decay_span) + far_level)


def shard_levels(key, extent, shards, smallest, top_value):
    def one(position, blocks):
        draws = jax.random.uniform(jax.random.fold_in(jax.random.fold_in(key, 6), position), (blocks,), jnp.float32, smallest / len(shards), top_value / len(shards))
        return jnp.repeat(jnp.exp(draws), extent[position] // blocks).reshape((-1,) + (1,) * (len(extent) - position - 1))

    level = one(*shards[0])
    for cut in shards[1:]:
        level = level * one(*cut)
    return level


def gaussian(key, shape, width, reach, cuts=(), kind=jnp.bfloat16):
    entries = width * jax.random.normal(key, shape, jnp.float32)
    if cuts:
        entries = entries * shard_levels(key, shape, cuts, -0.22, 0.18)
    return jnp.clip(entries, -reach, reach).astype(kind)


def setup_inputs(seed: int = 0) -> dict:
    splits = jax.random.split(jax.random.key(seed), 6)
    query_gate = gaussian(splits[0], (CHANNELS, LENGTH), 1.0, 6.0, ((0, 16), (1, 64)), jnp.float32)
    key_gate = gaussian(splits[1], (CHANNELS, LENGTH), 1.0, 6.0, ((0, 16), (1, 64)), jnp.float32)
    value_input = gaussian(splits[2], (CHANNELS, LENGTH), 1.0, 6.0, ((0, 16), (1, 64)), jnp.float32)
    filter_taps = draw_filter_taps(jax.random.fold_in(splits[5], 71), 0)
    cotangent = gaussian(splits[4], (CHANNELS, LENGTH), 1.0, 6.0, ((0, 16), (1, 64)), jnp.float32)
    return {"query_gate": query_gate, "key_gate": key_gate, "value_input": value_input, "filter_taps": filter_taps, "cotangent": cotangent}


def reference(query_gate, key_gate, value_input, filter_taps, cotangent):
    period = 2 * LENGTH
    spectra = jnp.fft.rfft(filter_taps, n=period, axis=-1)
    groups = CHANNELS // FILTERS

    def one_group(items):
        query_rows, key_rows, value_rows, grad_rows = items
        gated = key_rows * value_rows
        convolved = jnp.fft.irfft(jnp.fft.rfft(gated, n=period, axis=-1) * spectra, n=period, axis=-1)[:, :LENGTH]
        weighted = grad_rows * query_rows
        gated_grad = jnp.fft.irfft(jnp.fft.rfft(weighted, n=period, axis=-1) * jnp.conj(spectra), n=period, axis=-1)[:, :LENGTH]
        convolved = convolved.astype(jnp.float32)
        gated_grad = gated_grad.astype(jnp.float32)
        return grad_rows * convolved, gated_grad * value_rows, gated_grad * key_rows

    shaped = tuple(array.reshape(groups, FILTERS, LENGTH) for array in (query_gate, key_gate, value_input, cotangent))
    query_grad, key_grad, value_grad = lax.map(one_group, shaped)
    return (query_grad.reshape(CHANNELS, LENGTH), key_grad.reshape(CHANNELS, LENGTH), value_grad.reshape(CHANNELS, LENGTH))
```

```python
from functools import partial
import math

import jax
import jax.numpy as jnp
from jax import lax
from jax.sharding import PartitionSpec as P


def phase_table(row_count, column_count, offset, period, direction):
    row_index = lax.broadcasted_iota(jnp.int32, (row_count, column_count), 0)
    column_index = lax.broadcasted_iota(jnp.int32, (row_count, column_count), 1)
    phases = row_index * (column_index + offset) % period
    angles = phases.astype(jnp.float32) * (direction * 2.0 * math.pi / period)
    return (jnp.cos(angles), jnp.sin(angles))


def complex_mix(formula, table_real, table_imag, data_real, data_imag):
    product = partial(jnp.einsum, formula, precision=lax.Precision.HIGHEST)
    return (
        product(table_real, data_real) - product(table_imag, data_imag),
        product(table_real, data_imag) + product(table_imag, data_real),
    )


def regroup_tokens(signal):
    return lax.all_to_all(signal, "seq", split_axis=1, concat_axis=1, tiled=True)


def regroup_spectrum(part_real, part_imag):
    count = part_real.shape[0]
    moved = lax.all_to_all(
        jnp.concatenate([part_real, part_imag], axis=0),
        "seq",
        split_axis=1,
        concat_axis=1,
        tiled=True,
    )
    return moved[:count], moved[count:]


def finish_forward(moved_real, moved_imag, blocks, width, tokens):
    outer_real, outer_imag = phase_table(blocks, blocks, 0, blocks, -1.0)
    coarse_real, coarse_imag = complex_mix(
        "ur,crjq->cujq", outer_real, outer_imag, moved_real, moved_imag
    )
    shift_real, shift_imag = phase_table(blocks, width, 0, tokens, -1.0)
    shift_real = shift_real[None, :, None, :]
    shift_imag = shift_imag[None, :, None, :]
    twisted_real = coarse_real * shift_real - coarse_imag * shift_imag
    twisted_imag = coarse_real * shift_imag + coarse_imag * shift_real
    inner_real, inner_imag = phase_table(width, width, 0, width, -1.0)
    return complex_mix("qv,cujq->cujv", inner_real, inner_imag, twisted_real, twisted_imag)


def start_inverse(spectrum_real, spectrum_imag, blocks, width, tokens):
    inner_real, inner_imag = phase_table(width, width, 0, width, 1.0)
    fine_real, fine_imag = complex_mix(
        "vq,cujv->cujq", inner_real, inner_imag, spectrum_real, spectrum_imag
    )
    shift_real, shift_imag = phase_table(blocks, width, 0, tokens, 1.0)
    shift_real = shift_real[None, :, None, :]
    shift_imag = shift_imag[None, :, None, :]
    untwisted_real = fine_real * shift_real - fine_imag * shift_imag
    untwisted_imag = fine_real * shift_imag + fine_imag * shift_real
    outer_real, outer_imag = phase_table(blocks, blocks, 0, blocks, 1.0)
    return complex_mix("ru,cujq->crjq", outer_real, outer_imag, untwisted_real, untwisted_imag)


def forward_spectrum(signal):
    count, tokens = signal.shape
    blocks = lax.axis_size("seq")
    width = tokens // blocks
    freqs = 2 * blocks
    period = freqs * tokens
    rank = lax.axis_index("seq")
    gathered = regroup_tokens(signal.reshape(count, blocks, width))
    product = partial(jnp.einsum, "kp,cpq->ckq", precision=lax.Precision.HIGHEST)
    anchor = rank * width
    first_real, first_imag = phase_table(freqs, blocks, 0, freqs, -1.0)
    mixed_real = product(first_real, gathered)
    mixed_imag = product(first_imag, gathered)
    turn_real, turn_imag = phase_table(freqs, width, anchor, period, -1.0)
    moved_real, moved_imag = regroup_spectrum(
        mixed_real * turn_real - mixed_imag * turn_imag,
        mixed_real * turn_imag + mixed_imag * turn_real,
    )
    moved_real = moved_real.reshape(count, blocks, 2, width)
    moved_imag = moved_imag.reshape(count, blocks, 2, width)
    return finish_forward(moved_real, moved_imag, blocks, width, tokens)


def inverse_spectrum(spectrum_real, spectrum_imag):
    count, blocks, per_device, width = spectrum_real.shape
    tokens = blocks * width
    freqs = 2 * blocks
    period = freqs * tokens
    rank = lax.axis_index("seq")
    spread_real, spread_imag = start_inverse(spectrum_real, spectrum_imag, blocks, width, tokens)
    product = partial(jnp.einsum, "kp,ckq->cpq", precision=lax.Precision.HIGHEST)
    anchor = rank * width
    moved_real, moved_imag = regroup_spectrum(
        spread_real.reshape(count, blocks * per_device, width),
        spread_imag.reshape(count, blocks * per_device, width),
    )
    turn_real, turn_imag = phase_table(freqs, width, anchor, period, 1.0)
    level_real = moved_real * turn_real - moved_imag * turn_imag
    level_imag = moved_real * turn_imag + moved_imag * turn_real
    first_real, first_imag = phase_table(freqs, blocks, 0, freqs, 1.0)
    rebuilt = (product(first_real, level_real) - product(first_imag, level_imag)) * (1.0 / period)
    return regroup_tokens(rebuilt).reshape(count, tokens)


def on_device(query_gate, key_gate, value_input, filter_taps, cotangent):
    block_taps = lax.all_gather(filter_taps, "chan", axis=1, tiled=True)
    gated = key_gate * value_input
    weighted = cotangent * query_gate
    rows = gated.shape[0]
    filters = block_taps.shape[0]
    all_real, all_imag = forward_spectrum(
        jnp.concatenate([block_taps, gated, weighted], axis=0)
    )
    filter_real, filter_imag = all_real[:filters], all_imag[:filters]
    gated_real = all_real[filters:filters + rows]
    gated_imag = all_imag[filters:filters + rows]
    weighted_real = all_real[filters + rows:]
    weighted_imag = all_imag[filters + rows:]
    reps = rows // filters
    filter_real = jnp.tile(filter_real, (reps, 1, 1, 1))
    filter_imag = jnp.tile(filter_imag, (reps, 1, 1, 1))
    both = inverse_spectrum(
        jnp.concatenate(
            [
                gated_real * filter_real - gated_imag * filter_imag,
                weighted_real * filter_real + weighted_imag * filter_imag,
            ],
            axis=0,
        ),
        jnp.concatenate(
            [
                gated_real * filter_imag + gated_imag * filter_real,
                weighted_imag * filter_real - weighted_real * filter_imag,
            ],
            axis=0,
        ),
    )
    convolved = both[:rows]
    gated_grad = both[rows:]
    return (cotangent * convolved, gated_grad * value_input, gated_grad * key_gate)


def solution(mesh):
    in_specs = (
        P("chan", "seq"),
        P("chan", "seq"),
        P("chan", "seq"),
        P(None, ("seq", "chan")),
        P("chan", "seq"),
    )
    out_specs = (P("chan", "seq"), P("chan", "seq"), P("chan", "seq"))
    return jax.shard_map(
        on_device, mesh=mesh, in_specs=in_specs, out_specs=out_specs, check_vma=False
    )
```

```python
from functools import partial
import math

import jax
import jax.numpy as jnp
from jax import lax
from jax.sharding import PartitionSpec as P


def phase_table(row_count, column_count, offset, period, direction):
    row_index = lax.broadcasted_iota(jnp.int32, (row_count, column_count), 0)
    column_index = lax.broadcasted_iota(jnp.int32, (row_count, column_count), 1)
    phases = row_index * (column_index + offset) % period
    angles = phases.astype(jnp.float32) * (direction * 2.0 * math.pi / period)
    return (jnp.cos(angles), jnp.sin(angles))


def complex_mix(formula, table_real, table_imag, data_real, data_imag):
    product = partial(jnp.einsum, formula, precision=lax.Precision.HIGHEST)
    return (
        product(table_real, data_real) - product(table_imag, data_imag),
        product(table_real, data_imag) + product(table_imag, data_real),
    )


def regroup_tokens(signal):
    return lax.all_to_all(signal, "seq", split_axis=1, concat_axis=1, tiled=True)


def regroup_spectrum(part_real, part_imag):
    count = part_real.shape[0]
    moved = lax.all_to_all(
        jnp.concatenate([part_real, part_imag], axis=0),
        "seq",
        split_axis=1,
        concat_axis=1,
        tiled=True,
    )
    return moved[:count], moved[count:]


def finish_forward(moved_real, moved_imag, blocks, width, tokens):
    outer_real, outer_imag = phase_table(blocks, blocks, 0, blocks, -1.0)
    coarse_real, coarse_imag = complex_mix(
        "ur,crjq->cujq", outer_real, outer_imag, moved_real, moved_imag
    )
    shift_real, shift_imag = phase_table(blocks, width, 0, tokens, -1.0)
    shift_real = shift_real[None, :, None, :]
    shift_imag = shift_imag[None, :, None, :]
    twisted_real = coarse_real * shift_real - coarse_imag * shift_imag
    twisted_imag = coarse_real * shift_imag + coarse_imag * shift_real
    inner_real, inner_imag = phase_table(width, width, 0, width, -1.0)
    return complex_mix("qv,cujq->cujv", inner_real, inner_imag, twisted_real, twisted_imag)


def start_inverse(spectrum_real, spectrum_imag, blocks, width, tokens):
    inner_real, inner_imag = phase_table(width, width, 0, width, 1.0)
    fine_real, fine_imag = complex_mix(
        "vq,cujv->cujq", inner_real, inner_imag, spectrum_real, spectrum_imag
    )
    shift_real, shift_imag = phase_table(blocks, width, 0, tokens, 1.0)
    shift_real = shift_real[None, :, None, :]
    shift_imag = shift_imag[None, :, None, :]
    untwisted_real = fine_real * shift_real - fine_imag * shift_imag
    untwisted_imag = fine_real * shift_imag + fine_imag * shift_real
    outer_real, outer_imag = phase_table(blocks, blocks, 0, blocks, 1.0)
    return complex_mix("ru,cujq->crjq", outer_real, outer_imag, untwisted_real, untwisted_imag)


def column_twist(row, blocks, width, period, direction):
    column_index = lax.broadcasted_iota(jnp.int32, (blocks, width), 0) * width + lax.broadcasted_iota(
        jnp.int32, (blocks, width), 1
    )
    phases = row * column_index % period
    angles = phases.astype(jnp.float32) * (direction * 2.0 * math.pi / period)
    return (jnp.cos(angles), jnp.sin(angles))


def alternating(count, axis):
    index = lax.broadcasted_iota(jnp.int32, (count, count), axis)
    return (1 - 2 * (index % 2)).astype(jnp.float32)


def forward_spectrum(signal):
    count, tokens = signal.shape
    blocks = lax.axis_size("seq")
    width = tokens // blocks
    freqs = 2 * blocks
    period = freqs * tokens
    rank = lax.axis_index("seq")
    gathered = regroup_tokens(signal.reshape(count, blocks, width))
    product = partial(jnp.einsum, "kp,cpq->ckq", precision=lax.Precision.HIGHEST)
    anchor = rank * width
    first_real, first_imag = phase_table(blocks, blocks, 0, freqs, -1.0)
    top_row = lax.broadcasted_iota(jnp.int32, (blocks, blocks), 0) == 0
    first_real = jnp.where(top_row, 1.0, first_real)
    first_imag = jnp.where(top_row, alternating(blocks, 1), first_imag)
    mixed_real = product(first_real, gathered)
    mixed_imag = product(first_imag, gathered)
    turn_real, turn_imag = phase_table(blocks, width, anchor, period, -1.0)
    moved_real, moved_imag = regroup_spectrum(
        mixed_real * turn_real - mixed_imag * turn_imag,
        mixed_real * turn_imag + mixed_imag * turn_real,
    )
    lead = rank == 0
    edge_real, edge_imag = column_twist(blocks, blocks, width, period, -1.0)
    low_real = moved_real
    low_imag = jnp.where(lead, 0.0, moved_imag)
    high_real = jnp.where(lead, moved_imag * edge_real, 0.0)
    high_imag = jnp.where(lead, moved_imag * edge_imag, 0.0)
    return finish_forward(
        jnp.stack([low_real, high_real], axis=2),
        jnp.stack([low_imag, high_imag], axis=2),
        blocks,
        width,
        tokens,
    )


def inverse_spectrum(spectrum_real, spectrum_imag):
    count, blocks, per_device, width = spectrum_real.shape
    tokens = blocks * width
    freqs = 2 * blocks
    period = freqs * tokens
    rank = lax.axis_index("seq")
    spread_real, spread_imag = start_inverse(spectrum_real, spectrum_imag, blocks, width, tokens)
    own_real, own_imag = column_twist(rank, blocks, width, period, 1.0)
    edge_real, edge_imag = column_twist(blocks, blocks, width, period, 1.0)
    low_real = spread_real[:, :, 0] * own_real - spread_imag[:, :, 0] * own_imag
    low_imag = spread_real[:, :, 0] * own_imag + spread_imag[:, :, 0] * own_real
    high_real = spread_real[:, :, 1] * edge_real - spread_imag[:, :, 1] * edge_imag
    moved_real, moved_imag = regroup_spectrum(
        low_real, jnp.where(rank == 0, high_real, low_imag)
    )
    cos_table, sin_table = phase_table(blocks, blocks, 0, freqs, 1.0)
    first_column = lax.broadcasted_iota(jnp.int32, (blocks, blocks), 1) == 0
    real_weight = jnp.where(first_column, 1.0, 2.0 * cos_table)
    imag_weight = jnp.where(first_column, alternating(blocks, 0), -2.0 * sin_table)
    product = partial(jnp.einsum, "pk,ckq->cpq", precision=lax.Precision.HIGHEST)
    rebuilt = (product(real_weight, moved_real) + product(imag_weight, moved_imag)) * (1.0 / period)
    return regroup_tokens(rebuilt).reshape(count, tokens)


def on_device(query_gate, key_gate, value_input, filter_taps, cotangent):
    block_taps = lax.all_gather(filter_taps, "chan", axis=1, tiled=True)
    gated = key_gate * value_input
    weighted = cotangent * query_gate
    rows = gated.shape[0]
    filters = block_taps.shape[0]
    all_real, all_imag = forward_spectrum(
        jnp.concatenate([block_taps, gated, weighted], axis=0)
    )
    filter_real, filter_imag = all_real[:filters], all_imag[:filters]
    gated_real = all_real[filters:filters + rows]
    gated_imag = all_imag[filters:filters + rows]
    weighted_real = all_real[filters + rows:]
    weighted_imag = all_imag[filters + rows:]
    reps = rows // filters
    filter_real = jnp.tile(filter_real, (reps, 1, 1, 1))
    filter_imag = jnp.tile(filter_imag, (reps, 1, 1, 1))
    both = inverse_spectrum(
        jnp.concatenate(
            [
                gated_real * filter_real - gated_imag * filter_imag,
                weighted_real * filter_real + weighted_imag * filter_imag,
            ],
            axis=0,
        ),
        jnp.concatenate(
            [
                gated_real * filter_imag + gated_imag * filter_real,
                weighted_imag * filter_real - weighted_real * filter_imag,
            ],
            axis=0,
        ),
    )
    convolved = both[:rows]
    gated_grad = both[rows:]
    return (cotangent * convolved, gated_grad * value_input, gated_grad * key_gate)


def solution(mesh):
    in_specs = (
        P("chan", "seq"),
        P("chan", "seq"),
        P("chan", "seq"),
        P(None, ("seq", "chan")),
        P("chan", "seq"),
    )
    out_specs = (P("chan", "seq"), P("chan", "seq"), P("chan", "seq"))
    return jax.shard_map(
        on_device, mesh=mesh, in_specs=in_specs, out_specs=out_specs, check_vma=False
    )
```

```python
from functools import partial
import math

import jax
import jax.numpy as jnp
from jax import lax
from jax.sharding import PartitionSpec as P


def phase_table(row_count, column_count, offset, period, direction):
    row_index = lax.broadcasted_iota(jnp.int32, (row_count, column_count), 0)
    column_index = lax.broadcasted_iota(jnp.int32, (row_count, column_count), 1)
    phases = row_index * (column_index + offset) % period
    angles = phases.astype(jnp.float32) * (direction * 2.0 * math.pi / period)
    return (jnp.cos(angles), jnp.sin(angles))


def complex_mix(formula, table_real, table_imag, data_real, data_imag):
    product = partial(jnp.einsum, formula, precision=lax.Precision.HIGHEST)
    return (
        product(table_real, data_real) - product(table_imag, data_imag),
        product(table_real, data_imag) + product(table_imag, data_real),
    )


def regroup_tokens(signal):
    return lax.all_to_all(signal, "seq", split_axis=1, concat_axis=1, tiled=True)


def regroup_spectrum(part_real, part_imag):
    count = part_real.shape[0]
    moved = lax.all_to_all(
        jnp.concatenate([part_real, part_imag], axis=0),
        "seq",
        split_axis=1,
        concat_axis=1,
        tiled=True,
    )
    return moved[:count], moved[count:]


def finish_forward(moved_real, moved_imag, blocks, width, tokens):
    outer_real, outer_imag = phase_table(blocks, blocks, 0, blocks, -1.0)
    coarse_real, coarse_imag = complex_mix(
        "ur,crjq->cujq", outer_real, outer_imag, moved_real, moved_imag
    )
    shift_real, shift_imag = phase_table(blocks, width, 0, tokens, -1.0)
    shift_real = shift_real[None, :, None, :]
    shift_imag = shift_imag[None, :, None, :]
    twisted_real = coarse_real * shift_real - coarse_imag * shift_imag
    twisted_imag = coarse_real * shift_imag + coarse_imag * shift_real
    inner_real, inner_imag = phase_table(width, width, 0, width, -1.0)
    return complex_mix("qv,cujq->cujv", inner_real, inner_imag, twisted_real, twisted_imag)


def start_inverse(spectrum_real, spectrum_imag, blocks, width, tokens):
    inner_real, inner_imag = phase_table(width, width, 0, width, 1.0)
    fine_real, fine_imag = complex_mix(
        "vq,cujv->cujq", inner_real, inner_imag, spectrum_real, spectrum_imag
    )
    shift_real, shift_imag = phase_table(blocks, width, 0, tokens, 1.0)
    shift_real = shift_real[None, :, None, :]
    shift_imag = shift_imag[None, :, None, :]
    untwisted_real = fine_real * shift_real - fine_imag * shift_imag
    untwisted_imag = fine_real * shift_imag + fine_imag * shift_real
    outer_real, outer_imag = phase_table(blocks, blocks, 0, blocks, 1.0)
    return complex_mix("ru,cujq->crjq", outer_real, outer_imag, untwisted_real, untwisted_imag)


def column_twist(row, blocks, width, period, direction):
    column_index = lax.broadcasted_iota(jnp.int32, (blocks, width), 0) * width + lax.broadcasted_iota(
        jnp.int32, (blocks, width), 1
    )
    phases = row * column_index % period
    angles = phases.astype(jnp.float32) * (direction * 2.0 * math.pi / period)
    return (jnp.cos(angles), jnp.sin(angles))


def alternating(count, axis):
    index = lax.broadcasted_iota(jnp.int32, (count, count), axis)
    return (1 - 2 * (index % 2)).astype(jnp.float32)


def split_columns(moved_real, moved_imag, rank, blocks, width, tokens):
    period = 2 * blocks * tokens
    lead = rank == 0
    edge_real, edge_imag = column_twist(blocks, blocks, width, period, -1.0)
    low_real = moved_real
    low_imag = jnp.where(lead, 0.0, moved_imag)
    high_real = jnp.where(lead, moved_imag * edge_real, 0.0)
    high_imag = jnp.where(lead, moved_imag * edge_imag, 0.0)
    return finish_forward(
        jnp.stack([low_real, high_real], axis=2),
        jnp.stack([low_imag, high_imag], axis=2),
        blocks,
        width,
        tokens,
    )


def forward_spectrum(signal):
    count, tokens = signal.shape
    blocks = lax.axis_size("seq")
    width = tokens // blocks
    freqs = 2 * blocks
    period = freqs * tokens
    rank = lax.axis_index("seq")
    gathered = regroup_tokens(signal.reshape(count, blocks, width))
    product = partial(jnp.einsum, "kp,cpq->ckq", precision=lax.Precision.HIGHEST)
    anchor = rank * width
    first_real, first_imag = phase_table(blocks, blocks, 0, freqs, -1.0)
    top_row = lax.broadcasted_iota(jnp.int32, (blocks, blocks), 0) == 0
    first_real = jnp.where(top_row, 1.0, first_real)
    first_imag = jnp.where(top_row, alternating(blocks, 1), first_imag)
    mixed_real = product(first_real, gathered)
    mixed_imag = product(first_imag, gathered)
    turn_real, turn_imag = phase_table(blocks, width, anchor, period, -1.0)
    moved_real, moved_imag = regroup_spectrum(
        mixed_real * turn_real - mixed_imag * turn_imag,
        mixed_real * turn_imag + mixed_imag * turn_real,
    )
    return split_columns(moved_real, moved_imag, rank, blocks, width, tokens)


def filter_spectrum(taps, tokens):
    filters, piece = taps.shape
    blocks = lax.axis_size("seq")
    width = tokens // blocks
    freqs = 2 * blocks
    period = freqs * tokens
    rank = lax.axis_index("seq")
    column = lax.broadcasted_iota(jnp.int32, (blocks,), 0)
    angles = (rank * column % freqs).astype(jnp.float32) * (-2.0 * math.pi / freqs)
    weight_real = jnp.where(column == 0, 1.0, jnp.cos(angles))
    weight_imag = jnp.where(column == 0, (1 - 2 * (rank % 2)).astype(jnp.float32), jnp.sin(angles))
    parts = jnp.concatenate(
        [weight_real[:, None, None] * taps[None], weight_imag[:, None, None] * taps[None]], axis=1
    )
    summed = lax.psum_scatter(parts, "seq", scatter_dimension=0, tiled=True)
    full = lax.all_gather(summed, "chan", axis=2, tiled=True).reshape(2 * filters, blocks, width)
    own_real, own_imag = column_twist(rank, blocks, width, period, -1.0)
    base_real, base_imag = full[:filters], full[filters:]
    return split_columns(
        base_real * own_real - base_imag * own_imag,
        base_real * own_imag + base_imag * own_real,
        rank,
        blocks,
        width,
        tokens,
    )


def inverse_spectrum(spectrum_real, spectrum_imag):
    count, blocks, per_device, width = spectrum_real.shape
    tokens = blocks * width
    freqs = 2 * blocks
    period = freqs * tokens
    rank = lax.axis_index("seq")
    spread_real, spread_imag = start_inverse(spectrum_real, spectrum_imag, blocks, width, tokens)
    own_real, own_imag = column_twist(rank, blocks, width, period, 1.0)
    edge_real, edge_imag = column_twist(blocks, blocks, width, period, 1.0)
    low_real = spread_real[:, :, 0] * own_real - spread_imag[:, :, 0] * own_imag
    low_imag = spread_real[:, :, 0] * own_imag + spread_imag[:, :, 0] * own_real
    high_real = spread_real[:, :, 1] * edge_real - spread_imag[:, :, 1] * edge_imag
    moved_real, moved_imag = regroup_spectrum(
        low_real, jnp.where(rank == 0, high_real, low_imag)
    )
    cos_table, sin_table = phase_table(blocks, blocks, 0, freqs, 1.0)
    first_column = lax.broadcasted_iota(jnp.int32, (blocks, blocks), 1) == 0
    real_weight = jnp.where(first_column, 1.0, 2.0 * cos_table)
    imag_weight = jnp.where(first_column, alternating(blocks, 0), -2.0 * sin_table)
    product = partial(jnp.einsum, "pk,ckq->cpq", precision=lax.Precision.HIGHEST)
    rebuilt = (product(real_weight, moved_real) + product(imag_weight, moved_imag)) * (1.0 / period)
    return regroup_tokens(rebuilt).reshape(count, tokens)


def on_device(query_gate, key_gate, value_input, filter_taps, cotangent):
    gated = key_gate * value_input
    weighted = cotangent * query_gate
    rows, tokens = gated.shape
    filter_real, filter_imag = filter_spectrum(filter_taps, tokens)
    all_real, all_imag = forward_spectrum(jnp.concatenate([gated, weighted], axis=0))
    gated_real, gated_imag = all_real[:rows], all_imag[:rows]
    weighted_real, weighted_imag = all_real[rows:], all_imag[rows:]
    reps = rows // filter_real.shape[0]
    filter_real = jnp.tile(filter_real, (reps, 1, 1, 1))
    filter_imag = jnp.tile(filter_imag, (reps, 1, 1, 1))
    both = inverse_spectrum(
        jnp.concatenate(
            [
                gated_real * filter_real - gated_imag * filter_imag,
                weighted_real * filter_real + weighted_imag * filter_imag,
            ],
            axis=0,
        ),
        jnp.concatenate(
            [
                gated_real * filter_imag + gated_imag * filter_real,
                weighted_imag * filter_real - weighted_real * filter_imag,
            ],
            axis=0,
        ),
    )
    convolved = both[:rows]
    gated_grad = both[rows:]
    return (cotangent * convolved, gated_grad * value_input, gated_grad * key_gate)


def solution(mesh):
    in_specs = (
        P("chan", "seq"),
        P("chan", "seq"),
        P("chan", "seq"),
        P(None, ("seq", "chan")),
        P("chan", "seq"),
    )
    out_specs = (P("chan", "seq"), P("chan", "seq"), P("chan", "seq"))
    return jax.shard_map(
        on_device, mesh=mesh, in_specs=in_specs, out_specs=out_specs, check_vma=False
    )
```

```python
from functools import partial
import math

import jax
import jax.numpy as jnp
from jax import lax
from jax.sharding import PartitionSpec as P


def phase_table(row_count, column_count, offset, period, direction):
    row_index = lax.broadcasted_iota(jnp.int32, (row_count, column_count), 0)
    column_index = lax.broadcasted_iota(jnp.int32, (row_count, column_count), 1)
    phases = row_index * (column_index + offset) % period
    angles = phases.astype(jnp.float32) * (direction * 2.0 * math.pi / period)
    return (jnp.cos(angles), jnp.sin(angles))


def complex_mix(formula, table_real, table_imag, data_real, data_imag):
    product = partial(jnp.einsum, formula, precision=lax.Precision.HIGHEST)
    return (
        product(table_real, data_real) - product(table_imag, data_imag),
        product(table_real, data_imag) + product(table_imag, data_real),
    )


def regroup_tokens(signal):
    return lax.all_to_all(signal, "seq", split_axis=1, concat_axis=1, tiled=True)


def regroup_spectrum(part_real, part_imag):
    count = part_real.shape[0]
    moved = lax.all_to_all(
        jnp.concatenate([part_real, part_imag], axis=0),
        "seq",
        split_axis=1,
        concat_axis=1,
        tiled=True,
    )
    return moved[:count], moved[count:]


def finish_forward(moved_real, moved_imag, blocks, width, tokens):
    outer_real, outer_imag = phase_table(blocks, blocks, 0, blocks, -1.0)
    coarse_real, coarse_imag = complex_mix(
        "ur,crjq->cujq", outer_real, outer_imag, moved_real, moved_imag
    )
    shift_real, shift_imag = phase_table(blocks, width, 0, tokens, -1.0)
    shift_real = shift_real[None, :, None, :]
    shift_imag = shift_imag[None, :, None, :]
    twisted_real = coarse_real * shift_real - coarse_imag * shift_imag
    twisted_imag = coarse_real * shift_imag + coarse_imag * shift_real
    inner_real, inner_imag = phase_table(width, width, 0, width, -1.0)
    return complex_mix("qv,cujq->cujv", inner_real, inner_imag, twisted_real, twisted_imag)


def start_inverse(spectrum_real, spectrum_imag, blocks, width, tokens):
    inner_real, inner_imag = phase_table(width, width, 0, width, 1.0)
    fine_real, fine_imag = complex_mix(
        "vq,cujv->cujq", inner_real, inner_imag, spectrum_real, spectrum_imag
    )
    shift_real, shift_imag = phase_table(blocks, width, 0, tokens, 1.0)
    shift_real = shift_real[None, :, None, :]
    shift_imag = shift_imag[None, :, None, :]
    untwisted_real = fine_real * shift_real - fine_imag * shift_imag
    untwisted_imag = fine_real * shift_imag + fine_imag * shift_real
    outer_real, outer_imag = phase_table(blocks, blocks, 0, blocks, 1.0)
    return complex_mix("ru,cujq->crjq", outer_real, outer_imag, untwisted_real, untwisted_imag)


def column_twist(row, blocks, width, period, direction):
    column_index = lax.broadcasted_iota(jnp.int32, (blocks, width), 0) * width + lax.broadcasted_iota(
        jnp.int32, (blocks, width), 1
    )
    phases = row * column_index % period
    angles = phases.astype(jnp.float32) * (direction * 2.0 * math.pi / period)
    return (jnp.cos(angles), jnp.sin(angles))


def alternating(count, axis):
    index = lax.broadcasted_iota(jnp.int32, (count, count), axis)
    return (1 - 2 * (index % 2)).astype(jnp.float32)


def forward_spectrum(signal):
    count, tokens = signal.shape
    blocks = lax.axis_size("seq")
    width = tokens // blocks
    freqs = 2 * blocks
    period = freqs * tokens
    rank = lax.axis_index("seq")
    gathered = regroup_tokens(signal.reshape(count, blocks, width))
    product = partial(jnp.einsum, "kp,cpq->ckq", precision=lax.Precision.HIGHEST)
    anchor = rank * width
    first_real, first_imag = phase_table(blocks, blocks, 0, freqs, -1.0)
    top_row = lax.broadcasted_iota(jnp.int32, (blocks, blocks), 0) == 0
    first_real = jnp.where(top_row, 1.0, first_real)
    first_imag = jnp.where(top_row, alternating(blocks, 1), first_imag)
    mixed_real = product(first_real, gathered)
    mixed_imag = product(first_imag, gathered)
    turn_real, turn_imag = phase_table(blocks, width, anchor, period, -1.0)
    moved_real, moved_imag = regroup_spectrum(
        mixed_real * turn_real - mixed_imag * turn_imag,
        mixed_real * turn_imag + mixed_imag * turn_real,
    )
    return moved_real, moved_imag


def inverse_spectrum(spectrum_real, spectrum_imag, high_real):
    count, blocks, per_device, width = spectrum_real.shape
    tokens = blocks * width
    freqs = 2 * blocks
    period = freqs * tokens
    rank = lax.axis_index("seq")
    spread_real, spread_imag = start_inverse(spectrum_real, spectrum_imag, blocks, width, tokens)
    own_real, own_imag = column_twist(rank, blocks, width, period, 1.0)
    low_real = spread_real[:, :, 0] * own_real - spread_imag[:, :, 0] * own_imag
    low_imag = spread_real[:, :, 0] * own_imag + spread_imag[:, :, 0] * own_real
    moved_real, moved_imag = regroup_spectrum(
        low_real, jnp.where(rank == 0, high_real, low_imag)
    )
    cos_table, sin_table = phase_table(blocks, blocks, 0, freqs, 1.0)
    first_column = lax.broadcasted_iota(jnp.int32, (blocks, blocks), 1) == 0
    real_weight = jnp.where(first_column, 1.0, 2.0 * cos_table)
    imag_weight = jnp.where(first_column, alternating(blocks, 0), -2.0 * sin_table)
    product = partial(jnp.einsum, "pk,ckq->cpq", precision=lax.Precision.HIGHEST)
    rebuilt = (product(real_weight, moved_real) + product(imag_weight, moved_imag)) * (1.0 / period)
    return regroup_tokens(rebuilt).reshape(count, tokens)


def spectral_products(all_real, all_imag, filters, rows):
    filter_real, filter_imag = all_real[:filters], all_imag[:filters]
    gated_real = all_real[filters:filters + rows]
    gated_imag = all_imag[filters:filters + rows]
    weighted_real = all_real[filters + rows:]
    weighted_imag = all_imag[filters + rows:]
    reps = rows // filters
    filter_real = jnp.tile(filter_real, (reps, 1, 1, 1))
    filter_imag = jnp.tile(filter_imag, (reps, 1, 1, 1))
    product_real = jnp.concatenate(
        [
            gated_real * filter_real - gated_imag * filter_imag,
            weighted_real * filter_real + weighted_imag * filter_imag,
        ],
        axis=0,
    )
    product_imag = jnp.concatenate(
        [
            gated_real * filter_imag + gated_imag * filter_real,
            weighted_imag * filter_real - weighted_real * filter_imag,
        ],
        axis=0,
    )
    return product_real, product_imag


def on_device(query_gate, key_gate, value_input, filter_taps, cotangent):
    block_taps = lax.all_gather(filter_taps, "chan", axis=1, tiled=True)
    gated = key_gate * value_input
    weighted = cotangent * query_gate
    rows, tokens = gated.shape
    filters = block_taps.shape[0]
    blocks = lax.axis_size("seq")
    width = tokens // blocks
    period = 2 * blocks * tokens
    rank = lax.axis_index("seq")
    lead = rank == 0
    moved_real, moved_imag = forward_spectrum(
        jnp.concatenate([block_taps, gated, weighted], axis=0)
    )
    low_real, low_imag = finish_forward(
        moved_real[:, :, None],
        jnp.where(lead, 0.0, moved_imag)[:, :, None],
        blocks,
        width,
        tokens,
    )

    def edge_column():
        edge_real, edge_imag = column_twist(blocks, blocks, width, period, -1.0)
        high_real, high_imag = finish_forward(
            (moved_imag * edge_real)[:, :, None],
            (moved_imag * edge_imag)[:, :, None],
            blocks,
            width,
            tokens,
        )
        spread_real, spread_imag = start_inverse(
            *spectral_products(high_real, high_imag, filters, rows), blocks, width, tokens
        )
        back_real, back_imag = column_twist(blocks, blocks, width, period, 1.0)
        return spread_real[:, :, 0] * back_real - spread_imag[:, :, 0] * back_imag

    high = lax.cond(
        lead, edge_column, lambda: jnp.zeros((2 * rows, blocks, width), jnp.float32)
    )
    both = inverse_spectrum(*spectral_products(low_real, low_imag, filters, rows), high)
    convolved = both[:rows]
    gated_grad = both[rows:]
    return (cotangent * convolved, gated_grad * value_input, gated_grad * key_gate)


def solution(mesh):
    in_specs = (
        P("chan", "seq"),
        P("chan", "seq"),
        P("chan", "seq"),
        P(None, ("seq", "chan")),
        P("chan", "seq"),
    )
    out_specs = (P("chan", "seq"), P("chan", "seq"), P("chan", "seq"))
    return jax.shard_map(
        on_device, mesh=mesh, in_specs=in_specs, out_specs=out_specs, check_vma=False
    )
```

```python
from functools import partial
import math

import jax
import jax.numpy as jnp
from jax import lax
from jax.sharding import PartitionSpec as P


def phase_table(row_count, column_count, offset, period, direction):
    row_index = lax.broadcasted_iota(jnp.int32, (row_count, column_count), 0)
    column_index = lax.broadcasted_iota(jnp.int32, (row_count, column_count), 1)
    phases = row_index * (column_index + offset) % period
    angles = phases.astype(jnp.float32) * (direction * 2.0 * math.pi / period)
    return (jnp.cos(angles), jnp.sin(angles))


def complex_mix(formula, table_real, table_imag, data_real, data_imag):
    product = partial(jnp.einsum, formula, precision=lax.Precision.HIGHEST)
    return (
        product(table_real, data_real) - product(table_imag, data_imag),
        product(table_real, data_imag) + product(table_imag, data_real),
    )


def regroup_tokens(signal):
    return lax.all_to_all(signal, "seq", split_axis=1, concat_axis=1, tiled=True)


def regroup_spectrum(part_real, part_imag):
    count = part_real.shape[0]
    moved = lax.all_to_all(
        jnp.concatenate([part_real, part_imag], axis=0),
        "seq",
        split_axis=1,
        concat_axis=1,
        tiled=True,
    )
    return moved[:count], moved[count:]


def finish_forward(moved_real, moved_imag, blocks, width, tokens):
    outer_real, outer_imag = phase_table(blocks, blocks, 0, blocks, -1.0)
    coarse_real, coarse_imag = complex_mix(
        "ur,crjq->cujq", outer_real, outer_imag, moved_real, moved_imag
    )
    shift_real, shift_imag = phase_table(blocks, width, 0, tokens, -1.0)
    shift_real = shift_real[None, :, None, :]
    shift_imag = shift_imag[None, :, None, :]
    twisted_real = coarse_real * shift_real - coarse_imag * shift_imag
    twisted_imag = coarse_real * shift_imag + coarse_imag * shift_real
    inner_real, inner_imag = phase_table(width, width, 0, width, -1.0)
    return complex_mix("qv,cujq->cujv", inner_real, inner_imag, twisted_real, twisted_imag)


def start_inverse(spectrum_real, spectrum_imag, blocks, width, tokens):
    inner_real, inner_imag = phase_table(width, width, 0, width, 1.0)
    fine_real, fine_imag = complex_mix(
        "vq,cujv->cujq", inner_real, inner_imag, spectrum_real, spectrum_imag
    )
    shift_real, shift_imag = phase_table(blocks, width, 0, tokens, 1.0)
    shift_real = shift_real[None, :, None, :]
    shift_imag = shift_imag[None, :, None, :]
    untwisted_real = fine_real * shift_real - fine_imag * shift_imag
    untwisted_imag = fine_real * shift_imag + fine_imag * shift_real
    outer_real, outer_imag = phase_table(blocks, blocks, 0, blocks, 1.0)
    return complex_mix("ru,cujq->crjq", outer_real, outer_imag, untwisted_real, untwisted_imag)


def column_twist(row, blocks, width, period, direction):
    column_index = lax.broadcasted_iota(jnp.int32, (blocks, width), 0) * width + lax.broadcasted_iota(
        jnp.int32, (blocks, width), 1
    )
    phases = row * column_index % period
    angles = phases.astype(jnp.float32) * (direction * 2.0 * math.pi / period)
    return (jnp.cos(angles), jnp.sin(angles))


def alternating(count, axis):
    index = lax.broadcasted_iota(jnp.int32, (count, count), axis)
    return (1 - 2 * (index % 2)).astype(jnp.float32)


def forward_spectrum(signal):
    count, tokens = signal.shape
    blocks = lax.axis_size("seq")
    width = tokens // blocks
    freqs = 2 * blocks
    period = freqs * tokens
    rank = lax.axis_index("seq")
    gathered = regroup_tokens(signal.reshape(count, blocks, width))
    product = partial(jnp.einsum, "kp,cpq->ckq", precision=lax.Precision.HIGHEST)
    anchor = rank * width
    first_real, first_imag = phase_table(blocks, blocks, 0, freqs, -1.0)
    top_row = lax.broadcasted_iota(jnp.int32, (blocks, blocks), 0) == 0
    first_real = jnp.where(top_row, 1.0, first_real)
    first_imag = jnp.where(top_row, alternating(blocks, 1), first_imag)
    mixed_real = product(first_real, gathered)
    mixed_imag = product(first_imag, gathered)
    turn_real, turn_imag = phase_table(blocks, width, anchor, period, -1.0)
    moved_real, moved_imag = regroup_spectrum(
        mixed_real * turn_real - mixed_imag * turn_imag,
        mixed_real * turn_imag + mixed_imag * turn_real,
    )
    return moved_real, moved_imag


def inverse_spectrum(spectrum_real, spectrum_imag, high_real):
    count, blocks, per_device, width = spectrum_real.shape
    tokens = blocks * width
    freqs = 2 * blocks
    period = freqs * tokens
    rank = lax.axis_index("seq")
    spread_real, spread_imag = start_inverse(spectrum_real, spectrum_imag, blocks, width, tokens)
    own_real, own_imag = column_twist(rank, blocks, width, period, 1.0)
    low_real = spread_real[:, :, 0] * own_real - spread_imag[:, :, 0] * own_imag
    low_imag = spread_real[:, :, 0] * own_imag + spread_imag[:, :, 0] * own_real
    moved_real, moved_imag = regroup_spectrum(
        low_real, jnp.where(rank == 0, high_real, low_imag)
    )
    cos_table, sin_table = phase_table(blocks, blocks, 0, freqs, 1.0)
    first_column = lax.broadcasted_iota(jnp.int32, (blocks, blocks), 1) == 0
    real_weight = jnp.where(first_column, 1.0, 2.0 * cos_table)
    imag_weight = jnp.where(first_column, alternating(blocks, 0), -2.0 * sin_table)
    product = partial(jnp.einsum, "pk,ckq->cpq", precision=lax.Precision.HIGHEST)
    rebuilt = (product(real_weight, moved_real) + product(imag_weight, moved_imag)) * (1.0 / period)
    return regroup_tokens(rebuilt).reshape(count, tokens)


def spectral_products(all_real, all_imag, filters, rows):
    filter_real, filter_imag = all_real[:filters], all_imag[:filters]
    gated_real = all_real[filters:filters + rows]
    gated_imag = all_imag[filters:filters + rows]
    weighted_real = all_real[filters + rows:]
    weighted_imag = all_imag[filters + rows:]
    reps = rows // filters
    filter_real = jnp.tile(filter_real, (reps, 1, 1, 1))
    filter_imag = jnp.tile(filter_imag, (reps, 1, 1, 1))
    product_real = jnp.concatenate(
        [
            gated_real * filter_real - gated_imag * filter_imag,
            weighted_real * filter_real + weighted_imag * filter_imag,
        ],
        axis=0,
    )
    product_imag = jnp.concatenate(
        [
            gated_real * filter_imag + gated_imag * filter_real,
            weighted_imag * filter_real - weighted_real * filter_imag,
        ],
        axis=0,
    )
    return product_real, product_imag


def on_device(query_gate, key_gate, value_input, filter_taps, cotangent):
    peers = lax.axis_size("chan")
    copies = jnp.broadcast_to(filter_taps[None], (peers,) + filter_taps.shape)
    block_taps = jnp.moveaxis(
        lax.all_to_all(copies, "chan", split_axis=0, concat_axis=0, tiled=True), 0, 1
    ).reshape(filter_taps.shape[0], peers * filter_taps.shape[1])
    gated = key_gate * value_input
    weighted = cotangent * query_gate
    rows, tokens = gated.shape
    filters = block_taps.shape[0]
    blocks = lax.axis_size("seq")
    width = tokens // blocks
    period = 2 * blocks * tokens
    rank = lax.axis_index("seq")
    lead = rank == 0
    moved_real, moved_imag = forward_spectrum(
        jnp.concatenate([block_taps, gated, weighted], axis=0)
    )
    low_real, low_imag = finish_forward(
        moved_real[:, :, None],
        jnp.where(lead, 0.0, moved_imag)[:, :, None],
        blocks,
        width,
        tokens,
    )

    def edge_column():
        edge_real, edge_imag = column_twist(blocks, blocks, width, period, -1.0)
        high_real, high_imag = finish_forward(
            (moved_imag * edge_real)[:, :, None],
            (moved_imag * edge_imag)[:, :, None],
            blocks,
            width,
            tokens,
        )
        spread_real, spread_imag = start_inverse(
            *spectral_products(high_real, high_imag, filters, rows), blocks, width, tokens
        )
        back_real, back_imag = column_twist(blocks, blocks, width, period, 1.0)
        return spread_real[:, :, 0] * back_real - spread_imag[:, :, 0] * back_imag

    high = lax.cond(
        lead, edge_column, lambda: jnp.zeros((2 * rows, blocks, width), jnp.float32)
    )
    both = inverse_spectrum(*spectral_products(low_real, low_imag, filters, rows), high)
    convolved = both[:rows]
    gated_grad = both[rows:]
    return (cotangent * convolved, gated_grad * value_input, gated_grad * key_gate)


def solution(mesh):
    in_specs = (
        P("chan", "seq"),
        P("chan", "seq"),
        P("chan", "seq"),
        P(None, ("seq", "chan")),
        P("chan", "seq"),
    )
    out_specs = (P("chan", "seq"), P("chan", "seq"), P("chan", "seq"))
    return jax.shard_map(
        on_device, mesh=mesh, in_specs=in_specs, out_specs=out_specs, check_vma=False
    )
```

```python
from functools import partial
import math

import jax
import jax.numpy as jnp
from jax import lax
from jax.sharding import PartitionSpec as P


def phase_table(row_count, column_count, offset, period, direction):
    row_index = lax.broadcasted_iota(jnp.int32, (row_count, column_count), 0)
    column_index = lax.broadcasted_iota(jnp.int32, (row_count, column_count), 1)
    phases = row_index * (column_index + offset) % period
    angles = phases.astype(jnp.float32) * (direction * 2.0 * math.pi / period)
    return (jnp.cos(angles), jnp.sin(angles))


def complex_mix(formula, table_real, table_imag, data_real, data_imag):
    product = partial(jnp.einsum, formula, precision=lax.Precision.HIGHEST)
    return (
        product(table_real, data_real) - product(table_imag, data_imag),
        product(table_real, data_imag) + product(table_imag, data_real),
    )


def regroup_tokens(signal):
    return lax.all_to_all(signal, "seq", split_axis=1, concat_axis=1, tiled=True)


def regroup_spectrum(part_real, part_imag):
    count = part_real.shape[0]
    moved = lax.all_to_all(
        jnp.concatenate([part_real, part_imag], axis=0),
        "seq",
        split_axis=1,
        concat_axis=1,
        tiled=True,
    )
    return moved[:count], moved[count:]


def finish_forward(moved_real, moved_imag, blocks, width, tokens):
    outer_real, outer_imag = phase_table(blocks, blocks, 0, blocks, -1.0)
    coarse_real, coarse_imag = complex_mix(
        "ur,crjq->cujq", outer_real, outer_imag, moved_real, moved_imag
    )
    shift_real, shift_imag = phase_table(blocks, width, 0, tokens, -1.0)
    shift_real = shift_real[None, :, None, :]
    shift_imag = shift_imag[None, :, None, :]
    twisted_real = coarse_real * shift_real - coarse_imag * shift_imag
    twisted_imag = coarse_real * shift_imag + coarse_imag * shift_real
    inner_real, inner_imag = phase_table(width, width, 0, width, -1.0)
    return complex_mix("qv,cujq->cujv", inner_real, inner_imag, twisted_real, twisted_imag)


def start_inverse(spectrum_real, spectrum_imag, blocks, width, tokens):
    inner_real, inner_imag = phase_table(width, width, 0, width, 1.0)
    fine_real, fine_imag = complex_mix(
        "vq,cujv->cujq", inner_real, inner_imag, spectrum_real, spectrum_imag
    )
    shift_real, shift_imag = phase_table(blocks, width, 0, tokens, 1.0)
    shift_real = shift_real[None, :, None, :]
    shift_imag = shift_imag[None, :, None, :]
    untwisted_real = fine_real * shift_real - fine_imag * shift_imag
    untwisted_imag = fine_real * shift_imag + fine_imag * shift_real
    outer_real, outer_imag = phase_table(blocks, blocks, 0, blocks, 1.0)
    return complex_mix("ru,cujq->crjq", outer_real, outer_imag, untwisted_real, untwisted_imag)


def column_twist(row, blocks, width, period, direction):
    column_index = lax.broadcasted_iota(jnp.int32, (blocks, width), 0) * width + lax.broadcasted_iota(
        jnp.int32, (blocks, width), 1
    )
    phases = row * column_index % period
    angles = phases.astype(jnp.float32) * (direction * 2.0 * math.pi / period)
    return (jnp.cos(angles), jnp.sin(angles))


def alternating(count, axis):
    index = lax.broadcasted_iota(jnp.int32, (count, count), axis)
    return (1 - 2 * (index % 2)).astype(jnp.float32)


def forward_spectrum(signal):
    count, tokens = signal.shape
    blocks = lax.axis_size("seq")
    width = tokens // blocks
    freqs = 2 * blocks
    period = freqs * tokens
    rank = lax.axis_index("seq")
    gathered = regroup_tokens(signal.reshape(count, blocks, width))
    product = partial(jnp.einsum, "kp,cpq->ckq", precision=lax.Precision.HIGHEST)
    anchor = rank * width
    first_real, first_imag = phase_table(blocks, blocks, 0, freqs, -1.0)
    top_row = lax.broadcasted_iota(jnp.int32, (blocks, blocks), 0) == 0
    first_real = jnp.where(top_row, 1.0, first_real)
    first_imag = jnp.where(top_row, alternating(blocks, 1), first_imag)
    mixed_real = product(first_real, gathered)
    mixed_imag = product(first_imag, gathered)
    turn_real, turn_imag = phase_table(blocks, width, anchor, period, -1.0)
    moved_real, moved_imag = regroup_spectrum(
        mixed_real * turn_real - mixed_imag * turn_imag,
        mixed_real * turn_imag + mixed_imag * turn_real,
    )
    lead = rank == 0
    edge_real, edge_imag = column_twist(blocks, blocks, width, period, -1.0)
    low_real = moved_real
    low_imag = jnp.where(lead, 0.0, moved_imag)
    high_real = jnp.where(lead, moved_imag * edge_real, 0.0)
    high_imag = jnp.where(lead, moved_imag * edge_imag, 0.0)
    return finish_forward(
        jnp.stack([low_real, high_real], axis=2),
        jnp.stack([low_imag, high_imag], axis=2),
        blocks,
        width,
        tokens,
    )


def inverse_spectrum(spectrum_real, spectrum_imag):
    count, blocks, per_device, width = spectrum_real.shape
    tokens = blocks * width
    freqs = 2 * blocks
    period = freqs * tokens
    rank = lax.axis_index("seq")
    spread_real, spread_imag = start_inverse(spectrum_real, spectrum_imag, blocks, width, tokens)
    own_real, own_imag = column_twist(rank, blocks, width, period, 1.0)
    edge_real, edge_imag = column_twist(blocks, blocks, width, period, 1.0)
    low_real = spread_real[:, :, 0] * own_real - spread_imag[:, :, 0] * own_imag
    low_imag = spread_real[:, :, 0] * own_imag + spread_imag[:, :, 0] * own_real
    high_real = spread_real[:, :, 1] * edge_real - spread_imag[:, :, 1] * edge_imag
    moved_real, moved_imag = regroup_spectrum(
        low_real, jnp.where(rank == 0, high_real, low_imag)
    )
    cos_table, sin_table = phase_table(blocks, blocks, 0, freqs, 1.0)
    first_column = lax.broadcasted_iota(jnp.int32, (blocks, blocks), 1) == 0
    real_weight = jnp.where(first_column, 1.0, 2.0 * cos_table)
    imag_weight = jnp.where(first_column, alternating(blocks, 0), -2.0 * sin_table)
    product = partial(jnp.einsum, "pk,ckq->cpq", precision=lax.Precision.HIGHEST)
    rebuilt = (product(real_weight, moved_real) + product(imag_weight, moved_imag)) * (1.0 / period)
    return regroup_tokens(rebuilt).reshape(count, tokens)


def on_device(query_gate, key_gate, value_input, filter_taps, cotangent):
    peers = lax.axis_size("chan")
    copies = jnp.broadcast_to(filter_taps[None], (peers,) + filter_taps.shape)
    block_taps = jnp.moveaxis(
        lax.all_to_all(copies, "chan", split_axis=0, concat_axis=0, tiled=True), 0, 1
    ).reshape(filter_taps.shape[0], peers * filter_taps.shape[1])
    gated = key_gate * value_input
    weighted = cotangent * query_gate
    rows = gated.shape[0]
    filters = block_taps.shape[0]
    all_real, all_imag = forward_spectrum(
        jnp.concatenate([block_taps, gated, weighted], axis=0)
    )
    filter_real, filter_imag = all_real[:filters], all_imag[:filters]
    gated_real = all_real[filters:filters + rows]
    gated_imag = all_imag[filters:filters + rows]
    weighted_real = all_real[filters + rows:]
    weighted_imag = all_imag[filters + rows:]
    reps = rows // filters
    filter_real = jnp.tile(filter_real, (reps, 1, 1, 1))
    filter_imag = jnp.tile(filter_imag, (reps, 1, 1, 1))
    both = inverse_spectrum(
        jnp.concatenate(
            [
                gated_real * filter_real - gated_imag * filter_imag,
                weighted_real * filter_real + weighted_imag * filter_imag,
            ],
            axis=0,
        ),
        jnp.concatenate(
            [
                gated_real * filter_imag + gated_imag * filter_real,
                weighted_imag * filter_real - weighted_real * filter_imag,
            ],
            axis=0,
        ),
    )
    convolved = both[:rows]
    gated_grad = both[rows:]
    return (cotangent * convolved, gated_grad * value_input, gated_grad * key_gate)


def solution(mesh):
    in_specs = (
        P("chan", "seq"),
        P("chan", "seq"),
        P("chan", "seq"),
        P(None, ("seq", "chan")),
        P("chan", "seq"),
    )
    out_specs = (P("chan", "seq"), P("chan", "seq"), P("chan", "seq"))
    return jax.shard_map(
        on_device, mesh=mesh, in_specs=in_specs, out_specs=out_specs, check_vma=False
    )
```

```python
from functools import partial
import math

import jax
import jax.numpy as jnp
from jax import lax
from jax.sharding import PartitionSpec as P


def phase_table(row_count, column_count, offset, period, direction):
    row_index = lax.broadcasted_iota(jnp.int32, (row_count, column_count), 0)
    column_index = lax.broadcasted_iota(jnp.int32, (row_count, column_count), 1)
    phases = row_index * (column_index + offset) % period
    angles = phases.astype(jnp.float32) * (direction * 2.0 * math.pi / period)
    return (jnp.cos(angles), jnp.sin(angles))


def complex_mix(formula, table_real, table_imag, data_real, data_imag):
    product = partial(jnp.einsum, formula, precision=lax.Precision.HIGH)
    return (
        product(table_real, data_real) - product(table_imag, data_imag),
        product(table_real, data_imag) + product(table_imag, data_real),
    )


def regroup_tokens(signal):
    return lax.all_to_all(signal, "seq", split_axis=1, concat_axis=1, tiled=True)


def regroup_spectrum(part_real, part_imag):
    count = part_real.shape[0]
    moved = lax.all_to_all(
        jnp.concatenate([part_real, part_imag], axis=0),
        "seq",
        split_axis=1,
        concat_axis=1,
        tiled=True,
    )
    return moved[:count], moved[count:]


def finish_forward(moved_real, moved_imag, blocks, width, tokens):
    outer_real, outer_imag = phase_table(blocks, blocks, 0, blocks, -1.0)
    coarse_real, coarse_imag = complex_mix(
        "ur,crjq->cujq", outer_real, outer_imag, moved_real, moved_imag
    )
    shift_real, shift_imag = phase_table(blocks, width, 0, tokens, -1.0)
    shift_real = shift_real[None, :, None, :]
    shift_imag = shift_imag[None, :, None, :]
    twisted_real = coarse_real * shift_real - coarse_imag * shift_imag
    twisted_imag = coarse_real * shift_imag + coarse_imag * shift_real
    inner_real, inner_imag = phase_table(width, width, 0, width, -1.0)
    return complex_mix("qv,cujq->cujv", inner_real, inner_imag, twisted_real, twisted_imag)


def start_inverse(spectrum_real, spectrum_imag, blocks, width, tokens):
    inner_real, inner_imag = phase_table(width, width, 0, width, 1.0)
    fine_real, fine_imag = complex_mix(
        "vq,cujv->cujq", inner_real, inner_imag, spectrum_real, spectrum_imag
    )
    shift_real, shift_imag = phase_table(blocks, width, 0, tokens, 1.0)
    shift_real = shift_real[None, :, None, :]
    shift_imag = shift_imag[None, :, None, :]
    untwisted_real = fine_real * shift_real - fine_imag * shift_imag
    untwisted_imag = fine_real * shift_imag + fine_imag * shift_real
    outer_real, outer_imag = phase_table(blocks, blocks, 0, blocks, 1.0)
    return complex_mix("ru,cujq->crjq", outer_real, outer_imag, untwisted_real, untwisted_imag)


def column_twist(row, blocks, width, period, direction):
    column_index = lax.broadcasted_iota(jnp.int32, (blocks, width), 0) * width + lax.broadcasted_iota(
        jnp.int32, (blocks, width), 1
    )
    phases = row * column_index % period
    angles = phases.astype(jnp.float32) * (direction * 2.0 * math.pi / period)
    return (jnp.cos(angles), jnp.sin(angles))


def alternating(count, axis):
    index = lax.broadcasted_iota(jnp.int32, (count, count), axis)
    return (1 - 2 * (index % 2)).astype(jnp.float32)


def forward_spectrum(signal):
    count, tokens = signal.shape
    blocks = lax.axis_size("seq")
    width = tokens // blocks
    freqs = 2 * blocks
    period = freqs * tokens
    rank = lax.axis_index("seq")
    gathered = regroup_tokens(signal.reshape(count, blocks, width))
    product = partial(jnp.einsum, "kp,cpq->ckq", precision=lax.Precision.HIGH)
    anchor = rank * width
    first_real, first_imag = phase_table(blocks, blocks, 0, freqs, -1.0)
    top_row = lax.broadcasted_iota(jnp.int32, (blocks, blocks), 0) == 0
    first_real = jnp.where(top_row, 1.0, first_real)
    first_imag = jnp.where(top_row, alternating(blocks, 1), first_imag)
    mixed_real = product(first_real, gathered)
    mixed_imag = product(first_imag, gathered)
    turn_real, turn_imag = phase_table(blocks, width, anchor, period, -1.0)
    moved_real, moved_imag = regroup_spectrum(
        mixed_real * turn_real - mixed_imag * turn_imag,
        mixed_real * turn_imag + mixed_imag * turn_real,
    )
    return moved_real, moved_imag


def inverse_spectrum(spectrum_real, spectrum_imag, high_real):
    count, blocks, per_device, width = spectrum_real.shape
    tokens = blocks * width
    freqs = 2 * blocks
    period = freqs * tokens
    rank = lax.axis_index("seq")
    spread_real, spread_imag = start_inverse(spectrum_real, spectrum_imag, blocks, width, tokens)
    own_real, own_imag = column_twist(rank, blocks, width, period, 1.0)
    low_real = spread_real[:, :, 0] * own_real - spread_imag[:, :, 0] * own_imag
    low_imag = spread_real[:, :, 0] * own_imag + spread_imag[:, :, 0] * own_real
    moved_real, moved_imag = regroup_spectrum(
        low_real, jnp.where(rank == 0, high_real, low_imag)
    )
    cos_table, sin_table = phase_table(blocks, blocks, 0, freqs, 1.0)
    first_column = lax.broadcasted_iota(jnp.int32, (blocks, blocks), 1) == 0
    real_weight = jnp.where(first_column, 1.0, 2.0 * cos_table)
    imag_weight = jnp.where(first_column, alternating(blocks, 0), -2.0 * sin_table)
    product = partial(jnp.einsum, "pk,ckq->cpq", precision=lax.Precision.HIGH)
    rebuilt = (product(real_weight, moved_real) + product(imag_weight, moved_imag)) * (1.0 / period)
    return regroup_tokens(rebuilt).reshape(count, tokens)


def spectral_products(all_real, all_imag, filters, rows):
    filter_real, filter_imag = all_real[:filters], all_imag[:filters]
    gated_real = all_real[filters:filters + rows]
    gated_imag = all_imag[filters:filters + rows]
    weighted_real = all_real[filters + rows:]
    weighted_imag = all_imag[filters + rows:]
    reps = rows // filters
    filter_real = jnp.tile(filter_real, (reps, 1, 1, 1))
    filter_imag = jnp.tile(filter_imag, (reps, 1, 1, 1))
    product_real = jnp.concatenate(
        [
            gated_real * filter_real - gated_imag * filter_imag,
            weighted_real * filter_real + weighted_imag * filter_imag,
        ],
        axis=0,
    )
    product_imag = jnp.concatenate(
        [
            gated_real * filter_imag + gated_imag * filter_real,
            weighted_imag * filter_real - weighted_real * filter_imag,
        ],
        axis=0,
    )
    return product_real, product_imag


def on_device(query_gate, key_gate, value_input, filter_taps, cotangent):
    peers = lax.axis_size("chan")
    copies = jnp.broadcast_to(filter_taps[None], (peers,) + filter_taps.shape)
    block_taps = jnp.moveaxis(
        lax.all_to_all(copies, "chan", split_axis=0, concat_axis=0, tiled=True), 0, 1
    ).reshape(filter_taps.shape[0], peers * filter_taps.shape[1])
    gated = key_gate * value_input
    weighted = cotangent * query_gate
    rows, tokens = gated.shape
    filters = block_taps.shape[0]
    blocks = lax.axis_size("seq")
    width = tokens // blocks
    period = 2 * blocks * tokens
    rank = lax.axis_index("seq")
    lead = rank == 0
    moved_real, moved_imag = forward_spectrum(
        jnp.concatenate([block_taps, gated, weighted], axis=0)
    )
    low_real, low_imag = finish_forward(
        moved_real[:, :, None],
        jnp.where(lead, 0.0, moved_imag)[:, :, None],
        blocks,
        width,
        tokens,
    )

    def edge_column():
        edge_real, edge_imag = column_twist(blocks, blocks, width, period, -1.0)
        high_real, high_imag = finish_forward(
            (moved_imag * edge_real)[:, :, None],
            (moved_imag * edge_imag)[:, :, None],
            blocks,
            width,
            tokens,
        )
        spread_real, spread_imag = start_inverse(
            *spectral_products(high_real, high_imag, filters, rows), blocks, width, tokens
        )
        back_real, back_imag = column_twist(blocks, blocks, width, period, 1.0)
        return spread_real[:, :, 0] * back_real - spread_imag[:, :, 0] * back_imag

    high = lax.cond(
        lead, edge_column, lambda: jnp.zeros((2 * rows, blocks, width), jnp.float32)
    )
    both = inverse_spectrum(*spectral_products(low_real, low_imag, filters, rows), high)
    convolved = both[:rows]
    gated_grad = both[rows:]
    return (cotangent * convolved, gated_grad * value_input, gated_grad * key_gate)


def solution(mesh):
    in_specs = (
        P("chan", "seq"),
        P("chan", "seq"),
        P("chan", "seq"),
        P(None, ("seq", "chan")),
        P("chan", "seq"),
    )
    out_specs = (P("chan", "seq"), P("chan", "seq"), P("chan", "seq"))
    return jax.shard_map(
        on_device, mesh=mesh, in_specs=in_specs, out_specs=out_specs, check_vma=False
    )
```

```python
from functools import partial
import math

import jax
import jax.numpy as jnp
from jax import lax
from jax.sharding import PartitionSpec as P


def phase_table(row_count, column_count, offset, period, direction):
    row_index = lax.broadcasted_iota(jnp.int32, (row_count, column_count), 0)
    column_index = lax.broadcasted_iota(jnp.int32, (row_count, column_count), 1)
    phases = row_index * (column_index + offset) % period
    angles = phases.astype(jnp.float32) * (direction * 2.0 * math.pi / period)
    return (jnp.cos(angles), jnp.sin(angles))


def complex_mix(formula, table_real, table_imag, data_real, data_imag):
    product = partial(jnp.einsum, formula, precision=lax.Precision.HIGHEST)
    return (
        product(table_real, data_real) - product(table_imag, data_imag),
        product(table_real, data_imag) + product(table_imag, data_real),
    )


def regroup_tokens(signal):
    return lax.all_to_all(signal, "seq", split_axis=1, concat_axis=1, tiled=True)


def regroup_spectrum(part_real, part_imag):
    count = part_real.shape[0]
    moved = lax.all_to_all(
        jnp.concatenate([part_real, part_imag], axis=0),
        "seq",
        split_axis=1,
        concat_axis=1,
        tiled=True,
    )
    return moved[:count], moved[count:]


def finish_forward(moved_real, moved_imag, blocks, width, tokens):
    outer_real, outer_imag = phase_table(blocks, blocks, 0, blocks, -1.0)
    coarse_real, coarse_imag = complex_mix(
        "ur,crjq->cujq", outer_real, outer_imag, moved_real, moved_imag
    )
    shift_real, shift_imag = phase_table(blocks, width, 0, tokens, -1.0)
    shift_real = shift_real[None, :, None, :]
    shift_imag = shift_imag[None, :, None, :]
    twisted_real = coarse_real * shift_real - coarse_imag * shift_imag
    twisted_imag = coarse_real * shift_imag + coarse_imag * shift_real
    inner_real, inner_imag = phase_table(width, width, 0, width, -1.0)
    return complex_mix("qv,cujq->cujv", inner_real, inner_imag, twisted_real, twisted_imag)


def start_inverse(spectrum_real, spectrum_imag, blocks, width, tokens):
    inner_real, inner_imag = phase_table(width, width, 0, width, 1.0)
    fine_real, fine_imag = complex_mix(
        "vq,cujv->cujq", inner_real, inner_imag, spectrum_real, spectrum_imag
    )
    shift_real, shift_imag = phase_table(blocks, width, 0, tokens, 1.0)
    shift_real = shift_real[None, :, None, :]
    shift_imag = shift_imag[None, :, None, :]
    untwisted_real = fine_real * shift_real - fine_imag * shift_imag
    untwisted_imag = fine_real * shift_imag + fine_imag * shift_real
    outer_real, outer_imag = phase_table(blocks, blocks, 0, blocks, 1.0)
    return complex_mix("ru,cujq->crjq", outer_real, outer_imag, untwisted_real, untwisted_imag)


def column_twist(row, blocks, width, period, direction):
    column_index = lax.broadcasted_iota(jnp.int32, (blocks, width), 0) * width + lax.broadcasted_iota(
        jnp.int32, (blocks, width), 1
    )
    phases = row * column_index % period
    angles = phases.astype(jnp.float32) * (direction * 2.0 * math.pi / period)
    return (jnp.cos(angles), jnp.sin(angles))


def alternating(count, axis):
    index = lax.broadcasted_iota(jnp.int32, (count, count), axis)
    return (1 - 2 * (index % 2)).astype(jnp.float32)


def forward_spectrum(signal):
    count, tokens = signal.shape
    blocks = lax.axis_size("seq")
    width = tokens // blocks
    freqs = 2 * blocks
    period = freqs * tokens
    rank = lax.axis_index("seq")
    gathered = regroup_tokens(signal.reshape(count, blocks, width))
    product = partial(jnp.einsum, "kp,cpq->ckq", precision=lax.Precision.HIGH)
    anchor = rank * width
    first_real, first_imag = phase_table(blocks, blocks, 0, freqs, -1.0)
    top_row = lax.broadcasted_iota(jnp.int32, (blocks, blocks), 0) == 0
    first_real = jnp.where(top_row, 1.0, first_real)
    first_imag = jnp.where(top_row, alternating(blocks, 1), first_imag)
    mixed_real = product(first_real, gathered)
    mixed_imag = product(first_imag, gathered)
    turn_real, turn_imag = phase_table(blocks, width, anchor, period, -1.0)
    moved_real, moved_imag = regroup_spectrum(
        mixed_real * turn_real - mixed_imag * turn_imag,
        mixed_real * turn_imag + mixed_imag * turn_real,
    )
    return moved_real, moved_imag


def inverse_spectrum(spectrum_real, spectrum_imag, high_real):
    count, blocks, per_device, width = spectrum_real.shape
    tokens = blocks * width
    freqs = 2 * blocks
    period = freqs * tokens
    rank = lax.axis_index("seq")
    spread_real, spread_imag = start_inverse(spectrum_real, spectrum_imag, blocks, width, tokens)
    own_real, own_imag = column_twist(rank, blocks, width, period, 1.0)
    low_real = spread_real[:, :, 0] * own_real - spread_imag[:, :, 0] * own_imag
    low_imag = spread_real[:, :, 0] * own_imag + spread_imag[:, :, 0] * own_real
    moved_real, moved_imag = regroup_spectrum(
        low_real, jnp.where(rank == 0, high_real, low_imag)
    )
    cos_table, sin_table = phase_table(blocks, blocks, 0, freqs, 1.0)
    first_column = lax.broadcasted_iota(jnp.int32, (blocks, blocks), 1) == 0
    real_weight = jnp.where(first_column, 1.0, 2.0 * cos_table)
    imag_weight = jnp.where(first_column, alternating(blocks, 0), -2.0 * sin_table)
    product = partial(jnp.einsum, "pk,ckq->cpq", precision=lax.Precision.HIGH)
    rebuilt = (product(real_weight, moved_real) + product(imag_weight, moved_imag)) * (1.0 / period)
    return regroup_tokens(rebuilt).reshape(count, tokens)


def spectral_products(all_real, all_imag, filters, rows):
    filter_real, filter_imag = all_real[:filters], all_imag[:filters]
    gated_real = all_real[filters:filters + rows]
    gated_imag = all_imag[filters:filters + rows]
    weighted_real = all_real[filters + rows:]
    weighted_imag = all_imag[filters + rows:]
    reps = rows // filters
    filter_real = jnp.tile(filter_real, (reps, 1, 1, 1))
    filter_imag = jnp.tile(filter_imag, (reps, 1, 1, 1))
    product_real = jnp.concatenate(
        [
            gated_real * filter_real - gated_imag * filter_imag,
            weighted_real * filter_real + weighted_imag * filter_imag,
        ],
        axis=0,
    )
    product_imag = jnp.concatenate(
        [
            gated_real * filter_imag + gated_imag * filter_real,
            weighted_imag * filter_real - weighted_real * filter_imag,
        ],
        axis=0,
    )
    return product_real, product_imag


def on_device(query_gate, key_gate, value_input, filter_taps, cotangent):
    peers = lax.axis_size("chan")
    copies = jnp.broadcast_to(filter_taps[None], (peers,) + filter_taps.shape)
    block_taps = jnp.moveaxis(
        lax.all_to_all(copies, "chan", split_axis=0, concat_axis=0, tiled=True), 0, 1
    ).reshape(filter_taps.shape[0], peers * filter_taps.shape[1])
    gated = key_gate * value_input
    weighted = cotangent * query_gate
    rows, tokens = gated.shape
    filters = block_taps.shape[0]
    blocks = lax.axis_size("seq")
    width = tokens // blocks
    period = 2 * blocks * tokens
    rank = lax.axis_index("seq")
    lead = rank == 0
    moved_real, moved_imag = forward_spectrum(
        jnp.concatenate([block_taps, gated, weighted], axis=0)
    )
    low_real, low_imag = finish_forward(
        moved_real[:, :, None],
        jnp.where(lead, 0.0, moved_imag)[:, :, None],
        blocks,
        width,
        tokens,
    )

    def edge_column():
        edge_real, edge_imag = column_twist(blocks, blocks, width, period, -1.0)
        high_real, high_imag = finish_forward(
            (moved_imag * edge_real)[:, :, None],
            (moved_imag * edge_imag)[:, :, None],
            blocks,
            width,
            tokens,
        )
        spread_real, spread_imag = start_inverse(
            *spectral_products(high_real, high_imag, filters, rows), blocks, width, tokens
        )
        back_real, back_imag = column_twist(blocks, blocks, width, period, 1.0)
        return spread_real[:, :, 0] * back_real - spread_imag[:, :, 0] * back_imag

    high = lax.cond(
        lead, edge_column, lambda: jnp.zeros((2 * rows, blocks, width), jnp.float32)
    )
    both = inverse_spectrum(*spectral_products(low_real, low_imag, filters, rows), high)
    convolved = both[:rows]
    gated_grad = both[rows:]
    return (cotangent * convolved, gated_grad * value_input, gated_grad * key_gate)


def solution(mesh):
    in_specs = (
        P("chan", "seq"),
        P("chan", "seq"),
        P("chan", "seq"),
        P(None, ("seq", "chan")),
        P("chan", "seq"),
    )
    out_specs = (P("chan", "seq"), P("chan", "seq"), P("chan", "seq"))
    return jax.shard_map(
        on_device, mesh=mesh, in_specs=in_specs, out_specs=out_specs, check_vma=False
    )
```
